1024 devices in a mesh: tm: 32 (over x, y), ulysses: 32 (over z, core).
Axes of the slice: x: 4, y: 8, z: 16, core: 2. Of those that a mesh axis runs over, the one named last changes fastest.
Arguments:
- queries: bfloat16 [64, 64, 32, 1536], P('tm', None, 'ulysses'), may hold values from -24 to 24
- key_vectors: bfloat16 [64, 64, 32, 1536], P('tm', None, 'ulysses'), may hold values from -24 to 24
- value_vectors: bfloat16 [64, 64, 32, 1536], P('tm', None, 'ulysses'), may hold values from -6 to 6
- out_cotangent: bfloat16 [64, 64, 32, 1536], P('tm', None, 'ulysses'), may hold values from -6 to 6
- reach_time: int32 [12], replicated, may hold values from 0 to 1
- reach_height: int32 [12], replicated, may hold values from 0 to 1
- reach_width: int32 [12], replicated, may hold values from 0 to 3
Outputs:
- attention_out: bfloat16 [64, 64, 32, 1536], P('tm', None, 'ulysses')
- grad_queries: bfloat16 [64, 64, 32, 1536], P('tm', None, 'ulysses')
- grad_keys: bfloat16 [64, 64, 32, 1536], P('tm', None, 'ulysses')
- grad_values: bfloat16 [64, 64, 32, 1536], P('tm', None, 'ulysses')
The draws below stay inside these ranges and needn't reach their ends.
All inputs are finite; a program needn't handle non-finite values.
Results may differ from the reference program's by a relative error of at most 0.012.
The reference program's roundings to bfloat16 on the way (of `weights_b` and `grad_scores`) count: a program that leaves them out, or rounds other values in their place, can miss the bound.
Values may be sent and summed in bfloat16 or wider, within the bound.
No kernel may reach another device: no remote copies, remote signals or barrier semaphores. Data moves between devices by JAX's collectives and lax.ppermute only.
A program may use at most 64 MiB of HBM per device.

```python
import math
import jax
import jax.numpy as jnp
from jax import lax

DH = 128
HEADS = 12
TW = 8
FRAMES = 64
HEIGHT = 64
WIDTH = 32
FEAT = 1536


def drawn_parts(key):
    lead = (FRAMES, HEIGHT, WIDTH, HEADS)
    shape = lead + (DH,)
    base_q = jax.random.normal(jax.random.fold_in(key, 11), shape, jnp.float32)
    base_k = jax.random.normal(jax.random.fold_in(key, 12), shape, jnp.float32)
    flat = (FRAMES, HEIGHT, WIDTH, HEADS * DH)
    return (jnp.clip(base_q, -24.0, 24.0).reshape(flat), jnp.clip(base_k, -24.0, 24.0).reshape(flat))


def draw_queries(key, part):
    return drawn_parts(key)[0].astype(jnp.bfloat16)


def draw_key_vectors(key, part):
    return drawn_parts(key)[1].astype(jnp.bfloat16)


def place_ends(drawn, rng, smallest, largest):
    longest = drawn.shape.index(max(drawn.shape))
    spots = []
    for shift in (0, 1):
        where = [jax.random.randint(jax.random.fold_in(rng, axis), (), 0, length) for axis, length in enumerate(drawn.shape)]
        where[longest] = (where[longest] + shift) % drawn.shape[longest]
        spots.append(tuple(where))
    return drawn.at[spots[0]].set(smallest).at[spots[1]].set(largest)


def steps_of(stream_key, dims, pieces, least, high):
    loudness, own = 1.0, jax.random.fold_in(stream_key, 6)
    for dim, blocks in pieces:
        heights = jnp.exp(jax.random.uniform(jax.random.fold_in(own, dim), (blocks,), jnp.float32, least / len(pieces), high / len(pieces)))
        loudness = loudness * jnp.repeat(heights, dims[dim] // blocks).reshape([-1 if axis == dim else 1 for axis in range(len(dims))])
    return loudness


def bell_draw(own_key, shape, deviation, limit, pieces=(), held_as=jnp.bfloat16):
    values = jax.random.normal(own_key, shape, jnp.float32) * deviation
    if len(pieces) > 0:
        values = steps_of(own_key, shape, pieces, -0.22, 0.18) * values
    return jnp.clip(values, min=-limit, max=limit).astype(held_as)


def setup_inputs(seed: int = 0) -> dict:
    streams_of = jax.random.split(jax.random.key(seed), 8)
    queries = draw_queries(jax.random.fold_in(streams_of[7], 71), 0)
    key_vectors = draw_key_vectors(jax.random.fold_in(streams_of[7], 71), 0)
    value_vectors = bell_draw(streams_of[2], (FRAMES, HEIGHT, WIDTH, FEAT), 1.0, 6.0, ((0, 32), (2, 32)))
    out_cotangent = bell_draw(streams_of[3], (FRAMES, HEIGHT, WIDTH, FEAT), 1.0, 6.0, ((0, 32), (2, 32)))
    reach_time = place_ends(jax.random.randint(streams_of[4], (HEADS,), 0, 2), jax.random.fold_in(streams_of[4], 1), 0, 1).astype(jnp.int32)
    reach_height = place_ends(jax.random.randint(streams_of[5], (HEADS,), 0, 2), jax.random.fold_in(streams_of[5], 1), 0, 1).astype(jnp.int32)
    reach_width = place_ends(jax.random.randint(streams_of[6], (HEADS,), 0, 4), jax.random.fold_in(streams_of[6], 1), 0, 3).astype(jnp.int32)
    return dict(queries=queries, key_vectors=key_vectors, value_vectors=value_vectors, out_cotangent=out_cotangent, reach_time=reach_time, reach_height=reach_height, reach_width=reach_width)


def tile_window(query_cols, key_cols, gap_time, gap_rows, key_live, span_time, span_height, span_width):
    gap_width = jnp.abs(query_cols[:, None] // TW - key_cols[None, :] // TW)
    inside = (gap_time[None, None, :] <= span_time[:, None, None]) & (gap_rows[None, None, :] <= span_height[:, None, None]) & (gap_width[None] <= span_width[:, None, None])
    return inside & key_live[None, None, :]

def reference(queries, key_vectors, value_vectors, out_cotangent, reach_time, reach_height, reach_width):
    frames, height, col_count, features = queries.shape
    score_scale = 1.0 / math.sqrt(DH)
    zero_index = jnp.zeros((), jnp.int32)
    highest = lax.Precision.HIGHEST
    pad_grid = ((1, 1), (1, 1), (0, 0), (0, 0), (0, 0))

    def padded(tensor):
        return jnp.pad(tensor.reshape(frames, height, col_count, HEADS, DH), pad_grid)
    queries_p = padded(queries)
    keys_p = padded(key_vectors)
    values_p = padded(value_vectors)
    grads_p = padded(out_cotangent)
    near_cols = jnp.arange(col_count, dtype=jnp.int32)
    rim_cols = jnp.tile(near_cols, 9)
    step_time = jnp.repeat(jnp.arange(3, dtype=jnp.int32) - 1, 3 * col_count)
    step_rows = jnp.tile(jnp.repeat(jnp.arange(3, dtype=jnp.int32) - 1, col_count), 3)
    gap_time = jnp.abs(step_time)
    gap_rows = jnp.abs(step_rows)

    def locate(block_index):
        frame_now = block_index // height
        row_now = block_index % height
        rim_time = frame_now + step_time
        rim_row = row_now + step_rows
        rim_live = (rim_time >= 0) & (rim_time < frames) & (rim_row >= 0) & (rim_row < height)
        window = tile_window(near_cols, rim_cols, gap_time, gap_rows, rim_live, reach_time, reach_height, reach_width)
        return (frame_now, row_now, window)

    def own_slice(tensor, frame_now, row_now):
        sliced = lax.dynamic_slice(tensor, (frame_now + 1, row_now + 1, zero_index, zero_index, zero_index), (1, 1, col_count, HEADS, DH))
        return sliced.reshape(col_count, HEADS, DH).astype(jnp.float32)

    def rim_slice(tensor, frame_now, row_now):
        sliced = lax.dynamic_slice(tensor, (frame_now, row_now, zero_index, zero_index, zero_index), (3, 3, col_count, HEADS, DH))
        return sliced.reshape(9 * col_count, HEADS, DH).astype(jnp.float32)
    shaped = (col_count, HEADS * DH)

    def query_pass(block_index):
        frame_now, row_now, window = locate(block_index)
        q_now = own_slice(queries_p, frame_now, row_now)
        do_now = own_slice(grads_p, frame_now, row_now)
        k_rim = rim_slice(keys_p, frame_now, row_now)
        v_rim = rim_slice(values_p, frame_now, row_now)
        scores = jnp.einsum('qhd,khd->hqk', q_now, k_rim, precision=highest) * score_scale
        scores = jnp.where(window, scores, -jnp.inf)
        row_peak = lax.optimization_barrier(jnp.max(scores, axis=2, keepdims=True))
        log_total = row_peak + jnp.log(lax.optimization_barrier(jnp.sum(jnp.exp(scores - row_peak), axis=2, keepdims=True)))
        weights = jnp.exp(scores - log_total)
        weights_b = lax.optimization_barrier(weights.astype(jnp.bfloat16)).astype(jnp.float32)
        out_now = jnp.einsum('hqk,khd->qhd', weights_b, v_rim, precision=highest).astype(jnp.bfloat16)
        out_back = lax.optimization_barrier(out_now).astype(jnp.float32)
        row_dot = lax.optimization_barrier(jnp.sum(do_now * out_back, axis=2)).T
        grad_weights = jnp.einsum('qhd,khd->hqk', do_now, v_rim, precision=highest)
        grad_scores = (weights * (grad_weights - row_dot[:, :, None])).astype(jnp.bfloat16)
        grad_scores = lax.optimization_barrier(grad_scores).astype(jnp.float32)
        grad_q_now = (jnp.einsum('hqk,khd->qhd', grad_scores, k_rim, precision=highest) * score_scale).astype(jnp.bfloat16)
        return (out_now.reshape(shaped), grad_q_now.reshape(shaped), log_total[:, :, 0].T, row_dot.T)
    block_count = frames * height
    block_ids = jnp.arange(block_count, dtype=jnp.int32)
    outs, grad_qs, totals, dots = lax.map(query_pass, block_ids)
    pad_stats = ((1, 1), (1, 1), (0, 0), (0, 0))
    totals_p = jnp.pad(totals.reshape(frames, height, col_count, HEADS), pad_stats)
    dots_p = jnp.pad(dots.reshape(frames, height, col_count, HEADS), pad_stats)

    def stat_slice(tensor, frame_now, row_now):
        sliced = lax.dynamic_slice(tensor, (frame_now, row_now, zero_index, zero_index), (3, 3, col_count, HEADS))
        return sliced.reshape(9 * col_count, HEADS).T

    def key_pass(block_index):
        frame_now, row_now, window = locate(block_index)
        k_now = own_slice(keys_p, frame_now, row_now)
        v_now = own_slice(values_p, frame_now, row_now)
        q_rim = rim_slice(queries_p, frame_now, row_now)
        do_rim = rim_slice(grads_p, frame_now, row_now)
        total_rim = stat_slice(totals_p, frame_now, row_now)
        dot_rim = stat_slice(dots_p, frame_now, row_now)
        scores = jnp.einsum('khd,qhd->hkq', k_now, q_rim, precision=highest) * score_scale
        scores = jnp.where(window, scores, -jnp.inf)
        weights = jnp.exp(scores - total_rim[:, None, :])
        weights_b = lax.optimization_barrier(weights.astype(jnp.bfloat16)).astype(jnp.float32)
        grad_weights = jnp.einsum('khd,qhd->hkq', v_now, do_rim, precision=highest)
        grad_scores = (weights * (grad_weights - dot_rim[:, None, :])).astype(jnp.bfloat16)
        grad_scores = lax.optimization_barrier(grad_scores).astype(jnp.float32)
        grad_k_now = (jnp.einsum('hkq,qhd->khd', grad_scores, q_rim, precision=highest) * score_scale).astype(jnp.bfloat16)
        grad_v_now = jnp.einsum('hkq,qhd->khd', weights_b, do_rim, precision=highest).astype(jnp.bfloat16)
        return (grad_k_now.reshape(shaped), grad_v_now.reshape(shaped))
    grad_ks, grad_vs = lax.map(key_pass, block_ids)
    full = (frames, height, col_count, HEADS * DH)
    return (outs.reshape(full), grad_qs.reshape(full), grad_ks.reshape(full), grad_vs.reshape(full))
```

```python
import math

import jax
import jax.numpy as jnp
from jax import lax
from jax.experimental import pallas as pl
from jax.experimental.pallas import tpu as pltpu
from jax.sharding import PartitionSpec as P

DH = 128
HEADS = 12
TW = 8


def with_halo(array, sides, width):
    for axis, dim in sides:
        count, length = (lax.axis_size(axis), array.shape[dim])
        up = [(i, (i + 1) % count) for i in range(count - 1)]
        down = [(j, i) for i, j in up]
        last = lax.slice_in_dim(array, length - width, length, axis=dim)
        initial = lax.slice_in_dim(array, 0, width, axis=dim)
        before = lax.ppermute(last, axis, up)
        after = lax.ppermute(initial, axis, down)
        array = jnp.concatenate([before, array, after], axis=dim)
    return array


def window_mask(h, reach_ref, live_ref, own_frames, own_rows, cols, rim_frames, rim_rows):
    own_n = own_frames * own_rows * cols
    rim_n = rim_frames * rim_rows * cols
    own_i = lax.broadcasted_iota(jnp.int32, (own_n, rim_n), 0)
    rim_j = lax.broadcasted_iota(jnp.int32, (own_n, rim_n), 1)
    own_t = own_i // (own_rows * cols)
    own_r = (own_i // cols) % own_rows
    own_c = own_i % cols
    rim_t = rim_j // (rim_rows * cols) - 1
    rim_r = (rim_j // cols) % rim_rows - 1
    rim_c = rim_j % cols
    gap_t = jnp.abs(own_t - rim_t)
    gap_r = jnp.abs(own_r - rim_r)
    gap_w = jnp.abs(own_c // TW - rim_c // TW)
    inside = (
        (gap_t <= reach_ref[0, h])
        & (gap_r <= reach_ref[1, h])
        & (gap_w <= reach_ref[2, h])
    )
    return inside & (live_ref[...] > 0)


def make_query_kernel(dims):
    score_scale = 1.0 / math.sqrt(DH)

    def kernel(reach_ref, q_ref, do_ref, k_ref, v_ref, live_ref, og_ref, lse_ref, dot_ref):
        h = pl.program_id(0)
        window = window_mask(h, reach_ref, live_ref, *dims)
        q_now = q_ref[...]
        do_now = do_ref[...]
        k_rim = k_ref[...]
        v_rim = v_ref[...]
        nt = (((1,), (1,)), ((), ()))
        scores = lax.dot_general(q_now, k_rim, nt, preferred_element_type=jnp.float32) * score_scale
        scores = jnp.where(window, scores, -jnp.inf)
        row_peak = jnp.max(scores, axis=1, keepdims=True)
        log_total = row_peak + jnp.log(jnp.sum(jnp.exp(scores - row_peak), axis=1, keepdims=True))
        weights = jnp.exp(scores - log_total)
        weights_b = weights.astype(jnp.bfloat16)
        out_now = jnp.dot(weights_b, v_rim, preferred_element_type=jnp.float32).astype(jnp.bfloat16)
        row_dot = jnp.sum(
            do_now.astype(jnp.float32) * out_now.astype(jnp.float32), axis=1, keepdims=True
        )
        grad_weights = lax.dot_general(do_now, v_rim, nt, preferred_element_type=jnp.float32)
        grad_scores = (weights * (grad_weights - row_dot)).astype(jnp.bfloat16)
        grad_q = jnp.dot(grad_scores, k_rim, preferred_element_type=jnp.float32) * score_scale
        og_ref[0] = out_now
        og_ref[1] = grad_q.astype(jnp.bfloat16)
        lse_ref[...] = log_total
        dot_ref[...] = row_dot

    return kernel


def make_key_kernel(dims):
    score_scale = 1.0 / math.sqrt(DH)

    def kernel(reach_ref, k_ref, v_ref, q_ref, do_ref, lse_ref, dot_ref, live_ref, gkv_ref):
        h = pl.program_id(0)
        window = window_mask(h, reach_ref, live_ref, *dims)
        k_now = k_ref[...]
        v_now = v_ref[...]
        q_rim = q_ref[...]
        do_rim = do_ref[...]
        nt = (((1,), (1,)), ((), ()))
        scores = lax.dot_general(k_now, q_rim, nt, preferred_element_type=jnp.float32) * score_scale
        scores = jnp.where(window, scores, -jnp.inf)
        weights = jnp.exp(scores - lse_ref[...])
        weights_b = weights.astype(jnp.bfloat16)
        grad_weights = lax.dot_general(v_now, do_rim, nt, preferred_element_type=jnp.float32)
        grad_scores = (weights * (grad_weights - dot_ref[...])).astype(jnp.bfloat16)
        grad_k = jnp.dot(grad_scores, q_rim, preferred_element_type=jnp.float32) * score_scale
        grad_v = jnp.dot(weights_b, do_rim, preferred_element_type=jnp.float32)
        gkv_ref[0] = grad_k.astype(jnp.bfloat16)
        gkv_ref[1] = grad_v.astype(jnp.bfloat16)

    return kernel


def body(queries, key_vectors, value_vectors, out_cotangent, reach_time, reach_height, reach_width):
    lane_count = lax.axis_size("ulysses")
    band_index = lax.axis_index("ulysses")
    time_index = lax.axis_index("tm")
    time_count = lax.axis_size("tm")
    frames_dev, height = queries.shape[0], queries.shape[1]
    rows_dev = height // lane_count
    features = queries.shape[3]
    heads = features // DH
    stacked = jnp.stack([queries, key_vectors, value_vectors, out_cotangent])
    own = lax.all_to_all(stacked, "ulysses", split_axis=2, concat_axis=3, tiled=True)
    col_count = own.shape[3]
    rim = with_halo(own, (("tm", 1), ("ulysses", 2)), 1)
    rim_frames, rim_rows = frames_dev + 2, rows_dev + 2
    own_n = frames_dev * rows_dev * col_count
    rim_n = rim_frames * rim_rows * col_count
    own_flat = own.reshape(4, own_n, features)
    rim_flat = rim.reshape(4, rim_n, features)
    dims = (frames_dev, rows_dev, col_count, rim_frames, rim_rows)

    rim_pos = jnp.arange(rim_n, dtype=jnp.int32)
    frame_of = time_index * frames_dev + rim_pos // (rim_rows * col_count) - 1
    row_of = band_index * rows_dev + (rim_pos // col_count) % rim_rows - 1
    live = (
        (frame_of >= 0)
        & (frame_of < time_count * frames_dev)
        & (row_of >= 0)
        & (row_of < height)
    ).astype(jnp.int32).reshape(1, rim_n)
    reach = jnp.stack([reach_time, reach_height, reach_width]).astype(jnp.int32)

    def own_spec(which):
        return pl.BlockSpec((None, own_n, DH), lambda h, r: (which, 0, h))

    def rim_spec(which):
        return pl.BlockSpec((None, rim_n, DH), lambda h, r: (which, 0, h))

    live_spec = pl.BlockSpec((1, rim_n), lambda h, r: (0, 0))
    pair_spec = pl.BlockSpec((2, own_n, DH), lambda h, r: (0, 0, h))
    stat_spec = pl.BlockSpec((None, own_n, 1), lambda h, r: (h, 0, 0))

    og, lse, dots = pl.pallas_call(
        make_query_kernel(dims),
        grid_spec=pltpu.PrefetchScalarGridSpec(
            num_scalar_prefetch=1,
            grid=(heads,),
            in_specs=[own_spec(0), own_spec(3), rim_spec(1), rim_spec(2), live_spec],
            out_specs=[pair_spec, stat_spec, stat_spec],
        ),
        out_shape=[
            jax.ShapeDtypeStruct((2, own_n, features), jnp.bfloat16),
            jax.ShapeDtypeStruct((heads, own_n, 1), jnp.float32),
            jax.ShapeDtypeStruct((heads, own_n, 1), jnp.float32),
        ],
    )(reach, own_flat, own_flat, rim_flat, rim_flat, live)

    def back_to_columns(pair):
        shaped = pair.reshape(2, frames_dev, rows_dev, col_count, features)
        return lax.all_to_all(shaped, "ulysses", split_axis=3, concat_axis=2, tiled=True)

    og_back = back_to_columns(og)

    statistics = jnp.stack([lse, dots]).reshape(2, heads, frames_dev, rows_dev, col_count)
    stat_rim = with_halo(statistics, (("tm", 2), ("ulysses", 3)), 1).reshape(2, heads, 1, rim_n)
    stat_rim_spec = [
        pl.BlockSpec((None, None, 1, rim_n), lambda h, r, w=w: (w, h, 0, 0)) for w in range(2)
    ]
    gkv = pl.pallas_call(
        make_key_kernel(dims),
        grid_spec=pltpu.PrefetchScalarGridSpec(
            num_scalar_prefetch=1,
            grid=(heads,),
            in_specs=[own_spec(1), own_spec(2), rim_spec(0), rim_spec(3)]
            + stat_rim_spec
            + [live_spec],
            out_specs=pair_spec,
        ),
        out_shape=jax.ShapeDtypeStruct((2, own_n, features), jnp.bfloat16),
    )(reach, own_flat, own_flat, rim_flat, rim_flat, stat_rim, stat_rim, live)
    gkv_back = back_to_columns(gkv)
    return (og_back[0], og_back[1], gkv_back[0], gkv_back[1])


def solution(mesh):
    in_specs = (
        P("tm", None, "ulysses", None),
        P("tm", None, "ulysses", None),
        P("tm", None, "ulysses", None),
        P("tm", None, "ulysses", None),
        P(),
        P(),
        P(),
    )
    out_specs = (
        P("tm", None, "ulysses", None),
        P("tm", None, "ulysses", None),
        P("tm", None, "ulysses", None),
        P("tm", None, "ulysses", None),
    )
    return jax.shard_map(body, mesh=mesh, in_specs=in_specs, out_specs=out_specs, check_vma=False)
```

```python
import math

import jax
import jax.numpy as jnp
from jax import lax
from jax.experimental import pallas as pl
from jax.experimental.pallas import tpu as pltpu
from jax.sharding import PartitionSpec as P

DH = 128
HEADS = 12
TW = 8


def neighbour(array, shift_t, shift_u):
    time_count = lax.axis_size("tm")
    lane_count = lax.axis_size("ulysses")
    pairs = []
    for t in range(time_count):
        for u in range(lane_count):
            t_to, u_to = t + shift_t, u + shift_u
            if 0 <= t_to < time_count and 0 <= u_to < lane_count:
                pairs.append((t * lane_count + u, t_to * lane_count + u_to))
    return lax.ppermute(array, ("tm", "ulysses"), pairs)


def with_rim(array, frame_dim):
    row_dim = frame_dim + 1
    frames, rows = array.shape[frame_dim], array.shape[row_dim]

    def part(tensor, dim, lo, hi):
        return lax.slice_in_dim(tensor, lo, hi, axis=dim)

    first_f, last_f = part(array, frame_dim, 0, 1), part(array, frame_dim, frames - 1, frames)
    slabs = []
    for shift_t, edge in ((1, last_f), (-1, first_f)):
        first_r, last_r = part(edge, row_dim, 0, 1), part(edge, row_dim, rows - 1, rows)
        slabs.append(
            jnp.concatenate(
                [
                    neighbour(last_r, shift_t, 1),
                    neighbour(edge, shift_t, 0),
                    neighbour(first_r, shift_t, -1),
                ],
                axis=row_dim,
            )
        )
    first_r, last_r = part(array, row_dim, 0, 1), part(array, row_dim, rows - 1, rows)
    middle = jnp.concatenate(
        [neighbour(last_r, 0, 1), array, neighbour(first_r, 0, -1)], axis=row_dim
    )
    return jnp.concatenate([slabs[0], middle, slabs[1]], axis=frame_dim)


def window_mask(h, reach_ref, live_ref, own_frames, own_rows, cols, rim_frames, rim_rows):
    own_n = own_frames * own_rows * cols
    rim_n = rim_frames * rim_rows * cols
    own_i = lax.broadcasted_iota(jnp.int32, (own_n, rim_n), 0)
    rim_j = lax.broadcasted_iota(jnp.int32, (own_n, rim_n), 1)
    own_t = own_i // (own_rows * cols)
    own_r = (own_i // cols) % own_rows
    own_c = own_i % cols
    rim_t = rim_j // (rim_rows * cols) - 1
    rim_r = (rim_j // cols) % rim_rows - 1
    rim_c = rim_j % cols
    gap_t = jnp.abs(own_t - rim_t)
    gap_r = jnp.abs(own_r - rim_r)
    gap_w = jnp.abs(own_c // TW - rim_c // TW)
    inside = (
        (gap_t <= reach_ref[0, h])
        & (gap_r <= reach_ref[1, h])
        & (gap_w <= reach_ref[2, h])
    )
    return inside & (live_ref[...] > 0)


def make_query_kernel(dims):
    score_scale = 1.0 / math.sqrt(DH)

    def kernel(reach_ref, q_ref, do_ref, k_ref, v_ref, live_ref, og_ref, lse_ref, dot_ref):
        h = pl.program_id(0)
        window = window_mask(h, reach_ref, live_ref, *dims)
        q_now = q_ref[...]
        do_now = do_ref[...]
        k_rim = k_ref[...]
        v_rim = v_ref[...]
        nt = (((1,), (1,)), ((), ()))
        scores = lax.dot_general(q_now, k_rim, nt, preferred_element_type=jnp.float32) * score_scale
        scores = jnp.where(window, scores, -jnp.inf)
        row_peak = jnp.max(scores, axis=1, keepdims=True)
        log_total = row_peak + jnp.log(jnp.sum(jnp.exp(scores - row_peak), axis=1, keepdims=True))
        weights = jnp.exp(scores - log_total)
        weights_b = weights.astype(jnp.bfloat16)
        out_now = jnp.dot(weights_b, v_rim, preferred_element_type=jnp.float32).astype(jnp.bfloat16)
        row_dot = jnp.sum(
            do_now.astype(jnp.float32) * out_now.astype(jnp.float32), axis=1, keepdims=True
        )
        grad_weights = lax.dot_general(do_now, v_rim, nt, preferred_element_type=jnp.float32)
        grad_scores = (weights * (grad_weights - row_dot)).astype(jnp.bfloat16)
        grad_q = jnp.dot(grad_scores, k_rim, preferred_element_type=jnp.float32) * score_scale
        og_ref[0] = out_now
        og_ref[1] = grad_q.astype(jnp.bfloat16)
        lse_ref[...] = log_total
        dot_ref[...] = row_dot

    return kernel


def make_key_kernel(dims):
    score_scale = 1.0 / math.sqrt(DH)

    def kernel(reach_ref, k_ref, v_ref, q_ref, do_ref, lse_ref, dot_ref, live_ref, buf_ref, gkv_ref):
        h = pl.program_id(0)
        window = window_mask(h, reach_ref, live_ref, *dims)
        k_now = k_ref[...]
        v_now = v_ref[...]
        q_rim = q_ref[...]
        do_rim = do_ref[...]
        nt = (((1,), (1,)), ((), ()))
        scores = lax.dot_general(k_now, q_rim, nt, preferred_element_type=jnp.float32) * score_scale
        scores = jnp.where(window, scores, -jnp.inf)
        weights = jnp.exp(scores - lse_ref[...])
        weights_b = weights.astype(jnp.bfloat16)
        grad_weights = lax.dot_general(v_now, do_rim, nt, preferred_element_type=jnp.float32)
        grad_scores = (weights * (grad_weights - dot_ref[...])).astype(jnp.bfloat16)
        grad_k = jnp.dot(grad_scores, q_rim, preferred_element_type=jnp.float32) * score_scale
        grad_v = jnp.dot(weights_b, do_rim, preferred_element_type=jnp.float32)
        gkv_ref[0] = grad_k.astype(jnp.bfloat16)
        gkv_ref[1] = grad_v.astype(jnp.bfloat16)

    return kernel


def body(queries, key_vectors, value_vectors, out_cotangent, reach_time, reach_height, reach_width):
    lane_count = lax.axis_size("ulysses")
    band_index = lax.axis_index("ulysses")
    time_index = lax.axis_index("tm")
    time_count = lax.axis_size("tm")
    frames_dev, height = queries.shape[0], queries.shape[1]
    rows_dev = height // lane_count
    features = queries.shape[3]
    heads = features // DH
    stacked = jnp.stack([key_vectors, value_vectors, queries, out_cotangent])
    own = lax.all_to_all(stacked, "ulysses", split_axis=2, concat_axis=3, tiled=True)
    col_count = own.shape[3]
    rim_frames, rim_rows = frames_dev + 2, rows_dev + 2
    own_n = frames_dev * rows_dev * col_count
    rim_n = rim_frames * rim_rows * col_count
    kv_rim = with_rim(own[0:2], 1).reshape(2, rim_n, features)
    qd_rim = with_rim(own[2:4], 1).reshape(2, rim_n, features)
    own_flat = own.reshape(4, own_n, features)
    dims = (frames_dev, rows_dev, col_count, rim_frames, rim_rows)

    rim_pos = jnp.arange(rim_n, dtype=jnp.int32)
    frame_of = time_index * frames_dev + rim_pos // (rim_rows * col_count) - 1
    row_of = band_index * rows_dev + (rim_pos // col_count) % rim_rows - 1
    live = (
        (frame_of >= 0)
        & (frame_of < time_count * frames_dev)
        & (row_of >= 0)
        & (row_of < height)
    ).astype(jnp.int32).reshape(1, rim_n)
    reach = jnp.stack([reach_time, reach_height, reach_width]).astype(jnp.int32)

    def own_spec(which):
        return pl.BlockSpec((None, own_n, DH), lambda h, r: (which, 0, h))

    def rim_spec(which):
        return pl.BlockSpec((None, rim_n, DH), lambda h, r: (which, 0, h))

    def pair_spec(which):
        return pl.BlockSpec((2, own_n, DH), lambda h, r: (which, 0, h))

    live_spec = pl.BlockSpec((1, rim_n), lambda h, r: (0, 0))
    stat_spec = pl.BlockSpec((None, own_n, 1), lambda h, r: (h, 0, 0))

    results, lse, dots = pl.pallas_call(
        make_query_kernel(dims),
        grid_spec=pltpu.PrefetchScalarGridSpec(
            num_scalar_prefetch=1,
            grid=(heads,),
            in_specs=[own_spec(2), own_spec(3), rim_spec(0), rim_spec(1), live_spec],
            out_specs=[pair_spec(0), stat_spec, stat_spec],
        ),
        out_shape=[
            jax.ShapeDtypeStruct((4, own_n, features), jnp.bfloat16),
            jax.ShapeDtypeStruct((heads, own_n, 1), jnp.float32),
            jax.ShapeDtypeStruct((heads, own_n, 1), jnp.float32),
        ],
    )(reach, own_flat, own_flat, kv_rim, kv_rim, live)

    statistics = jnp.stack([lse, dots]).reshape(2, heads, frames_dev, rows_dev, col_count)
    stat_rim = with_rim(statistics, 2).reshape(2, heads, 1, rim_n)
    stat_rim_spec = [
        pl.BlockSpec((None, None, 1, rim_n), lambda h, r, w=w: (w, h, 0, 0)) for w in range(2)
    ]
    results = pl.pallas_call(
        make_key_kernel(dims),
        grid_spec=pltpu.PrefetchScalarGridSpec(
            num_scalar_prefetch=1,
            grid=(heads,),
            in_specs=[own_spec(0), own_spec(1), rim_spec(0), rim_spec(1)]
            + stat_rim_spec
            + [live_spec, pl.BlockSpec(memory_space=pl.ANY)],
            out_specs=pair_spec(1),
        ),
        out_shape=jax.ShapeDtypeStruct((4, own_n, features), jnp.bfloat16),
        input_output_aliases={8: 0},
    )(reach, own_flat, own_flat, qd_rim, qd_rim, stat_rim, stat_rim, live, results)
    shaped = results.reshape(4, frames_dev, rows_dev, col_count, features)
    back = lax.all_to_all(shaped, "ulysses", split_axis=3, concat_axis=2, tiled=True)
    return (back[0], back[1], back[2], back[3])


def solution(mesh):
    in_specs = (
        P("tm", None, "ulysses", None),
        P("tm", None, "ulysses", None),
        P("tm", None, "ulysses", None),
        P("tm", None, "ulysses", None),
        P(),
        P(),
        P(),
    )
    out_specs = (
        P("tm", None, "ulysses", None),
        P("tm", None, "ulysses", None),
        P("tm", None, "ulysses", None),
        P("tm", None, "ulysses", None),
    )
    return jax.shard_map(body, mesh=mesh, in_specs=in_specs, out_specs=out_specs, check_vma=False)
```

```python
import math

import jax
import jax.numpy as jnp
from jax import lax
from jax.experimental import pallas as pl
from jax.experimental.pallas import tpu as pltpu
from jax.sharding import PartitionSpec as P

DH = 128
HEADS = 12
TW = 8
CHUNKS = 2


def with_halo(array, sides, width):
    for axis, dim in sides:
        count, length = (lax.axis_size(axis), array.shape[dim])
        up = [(i, (i + 1) % count) for i in range(count - 1)]
        down = [(j, i) for i, j in up]
        last = lax.slice_in_dim(array, length - width, length, axis=dim)
        initial = lax.slice_in_dim(array, 0, width, axis=dim)
        before = lax.ppermute(last, axis, up)
        after = lax.ppermute(initial, axis, down)
        array = jnp.concatenate([before, array, after], axis=dim)
    return array


def window_mask(h, reach_ref, live_ref, own_frames, own_rows, cols, rim_frames, rim_rows):
    own_n = own_frames * own_rows * cols
    rim_n = rim_frames * rim_rows * cols
    own_i = lax.broadcasted_iota(jnp.int32, (own_n, rim_n), 0)
    rim_j = lax.broadcasted_iota(jnp.int32, (own_n, rim_n), 1)
    own_t = own_i // (own_rows * cols)
    own_r = (own_i // cols) % own_rows
    own_c = own_i % cols
    rim_t = rim_j // (rim_rows * cols) - 1
    rim_r = (rim_j // cols) % rim_rows - 1
    rim_c = rim_j % cols
    gap_t = jnp.abs(own_t - rim_t)
    gap_r = jnp.abs(own_r - rim_r)
    gap_w = jnp.abs(own_c // TW - rim_c // TW)
    inside = (
        (gap_t <= reach_ref[0, h])
        & (gap_r <= reach_ref[1, h])
        & (gap_w <= reach_ref[2, h])
    )
    return inside & (live_ref[...] > 0)


def make_query_kernel(dims):
    score_scale = 1.0 / math.sqrt(DH)

    def kernel(reach_ref, q_ref, do_ref, k_ref, v_ref, live_ref, og_ref, lse_ref, dot_ref):
        h = pl.program_id(0)
        window = window_mask(h, reach_ref, live_ref, *dims)
        q_now = q_ref[...]
        do_now = do_ref[...]
        k_rim = k_ref[...]
        v_rim = v_ref[...]
        nt = (((1,), (1,)), ((), ()))
        scores = lax.dot_general(q_now, k_rim, nt, preferred_element_type=jnp.float32) * score_scale
        scores = jnp.where(window, scores, -jnp.inf)
        row_peak = jnp.max(scores, axis=1, keepdims=True)
        log_total = row_peak + jnp.log(jnp.sum(jnp.exp(scores - row_peak), axis=1, keepdims=True))
        weights = jnp.exp(scores - log_total)
        weights_b = weights.astype(jnp.bfloat16)
        out_now = jnp.dot(weights_b, v_rim, preferred_element_type=jnp.float32).astype(jnp.bfloat16)
        row_dot = jnp.sum(
            do_now.astype(jnp.float32) * out_now.astype(jnp.float32), axis=1, keepdims=True
        )
        grad_weights = lax.dot_general(do_now, v_rim, nt, preferred_element_type=jnp.float32)
        grad_scores = (weights * (grad_weights - row_dot)).astype(jnp.bfloat16)
        grad_q = jnp.dot(grad_scores, k_rim, preferred_element_type=jnp.float32) * score_scale
        og_ref[0] = out_now
        og_ref[1] = grad_q.astype(jnp.bfloat16)
        lse_ref[...] = log_total
        dot_ref[...] = row_dot

    return kernel


def make_key_kernel(dims):
    score_scale = 1.0 / math.sqrt(DH)

    def kernel(reach_ref, k_ref, v_ref, q_ref, do_ref, lse_ref, dot_ref, live_ref, gkv_ref):
        h = pl.program_id(0)
        window = window_mask(h, reach_ref, live_ref, *dims)
        k_now = k_ref[...]
        v_now = v_ref[...]
        q_rim = q_ref[...]
        do_rim = do_ref[...]
        nt = (((1,), (1,)), ((), ()))
        scores = lax.dot_general(k_now, q_rim, nt, preferred_element_type=jnp.float32) * score_scale
        scores = jnp.where(window, scores, -jnp.inf)
        weights = jnp.exp(scores - lse_ref[...])
        weights_b = weights.astype(jnp.bfloat16)
        grad_weights = lax.dot_general(v_now, do_rim, nt, preferred_element_type=jnp.float32)
        grad_scores = (weights * (grad_weights - dot_ref[...])).astype(jnp.bfloat16)
        grad_k = jnp.dot(grad_scores, q_rim, preferred_element_type=jnp.float32) * score_scale
        grad_v = jnp.dot(weights_b, do_rim, preferred_element_type=jnp.float32)
        gkv_ref[0] = grad_k.astype(jnp.bfloat16)
        gkv_ref[1] = grad_v.astype(jnp.bfloat16)

    return kernel


def attend(stacked, reach, time_index, band_index, time_count, height):
    frames_dev = stacked.shape[1]
    features = stacked.shape[4]
    heads = features // DH
    own = lax.all_to_all(stacked, "ulysses", split_axis=2, concat_axis=3, tiled=True)
    rows_dev, col_count = own.shape[2], own.shape[3]
    rim = with_halo(own, (("tm", 1), ("ulysses", 2)), 1)
    rim_frames, rim_rows = frames_dev + 2, rows_dev + 2
    own_n = frames_dev * rows_dev * col_count
    rim_n = rim_frames * rim_rows * col_count
    own_flat = own.reshape(4, own_n, features)
    rim_flat = rim.reshape(4, rim_n, features)
    dims = (frames_dev, rows_dev, col_count, rim_frames, rim_rows)

    rim_pos = jnp.arange(rim_n, dtype=jnp.int32)
    frame_of = time_index * frames_dev + rim_pos // (rim_rows * col_count) - 1
    row_of = band_index * rows_dev + (rim_pos // col_count) % rim_rows - 1
    live = (
        (frame_of >= 0)
        & (frame_of < time_count * frames_dev)
        & (row_of >= 0)
        & (row_of < height)
    ).astype(jnp.int32).reshape(1, rim_n)

    def own_spec(which):
        return pl.BlockSpec((None, own_n, DH), lambda h, r: (which, 0, h))

    def rim_spec(which):
        return pl.BlockSpec((None, rim_n, DH), lambda h, r: (which, 0, h))

    live_spec = pl.BlockSpec((1, rim_n), lambda h, r: (0, 0))
    pair_spec = pl.BlockSpec((2, own_n, DH), lambda h, r: (0, 0, h))
    stat_spec = pl.BlockSpec((None, own_n, 1), lambda h, r: (h, 0, 0))

    og, lse, dots = pl.pallas_call(
        make_query_kernel(dims),
        grid_spec=pltpu.PrefetchScalarGridSpec(
            num_scalar_prefetch=1,
            grid=(heads,),
            in_specs=[own_spec(0), own_spec(3), rim_spec(1), rim_spec(2), live_spec],
            out_specs=[pair_spec, stat_spec, stat_spec],
        ),
        out_shape=[
            jax.ShapeDtypeStruct((2, own_n, features), jnp.bfloat16),
            jax.ShapeDtypeStruct((heads, own_n, 1), jnp.float32),
            jax.ShapeDtypeStruct((heads, own_n, 1), jnp.float32),
        ],
    )(reach, own_flat, own_flat, rim_flat, rim_flat, live)

    def back_to_columns(pair):
        shaped = pair.reshape(2, frames_dev, rows_dev, col_count, features)
        return lax.all_to_all(shaped, "ulysses", split_axis=3, concat_axis=2, tiled=True)

    og_back = back_to_columns(og)

    statistics = jnp.stack([lse, dots]).reshape(2, heads, frames_dev, rows_dev, col_count)
    stat_rim = with_halo(statistics, (("tm", 2), ("ulysses", 3)), 1).reshape(2, heads, 1, rim_n)
    stat_rim_spec = [
        pl.BlockSpec((None, None, 1, rim_n), lambda h, r, w=w: (w, h, 0, 0)) for w in range(2)
    ]
    gkv = pl.pallas_call(
        make_key_kernel(dims),
        grid_spec=pltpu.PrefetchScalarGridSpec(
            num_scalar_prefetch=1,
            grid=(heads,),
            in_specs=[own_spec(1), own_spec(2), rim_spec(0), rim_spec(3)]
            + stat_rim_spec
            + [live_spec],
            out_specs=pair_spec,
        ),
        out_shape=jax.ShapeDtypeStruct((2, own_n, features), jnp.bfloat16),
    )(reach, own_flat, own_flat, rim_flat, rim_flat, stat_rim, stat_rim, live)
    gkv_back = back_to_columns(gkv)
    return (og_back[0], og_back[1], gkv_back[0], gkv_back[1])


def body(queries, key_vectors, value_vectors, out_cotangent, reach_time, reach_height, reach_width):
    band_index = lax.axis_index("ulysses")
    time_index = lax.axis_index("tm")
    time_count = lax.axis_size("tm")
    height = queries.shape[1]
    features = queries.shape[3]
    heads = features // DH
    chunk_heads = heads // CHUNKS
    width = chunk_heads * DH
    reach = jnp.stack([reach_time, reach_height, reach_width]).astype(jnp.int32)
    stacked = jnp.stack([queries, key_vectors, value_vectors, out_cotangent])
    pieces = []
    for chunk in range(CHUNKS):
        part = lax.slice_in_dim(stacked, chunk * width, (chunk + 1) * width, axis=4)
        part_reach = lax.slice_in_dim(reach, chunk * chunk_heads, (chunk + 1) * chunk_heads, axis=1)
        pieces.append(attend(part, part_reach, time_index, band_index, time_count, height))
    return tuple(jnp.concatenate([piece[i] for piece in pieces], axis=3) for i in range(4))


def solution(mesh):
    in_specs = (
        P("tm", None, "ulysses", None),
        P("tm", None, "ulysses", None),
        P("tm", None, "ulysses", None),
        P("tm", None, "ulysses", None),
        P(),
        P(),
        P(),
    )
    out_specs = (
        P("tm", None, "ulysses", None),
        P("tm", None, "ulysses", None),
        P("tm", None, "ulysses", None),
        P("tm", None, "ulysses", None),
    )
    return jax.shard_map(body, mesh=mesh, in_specs=in_specs, out_specs=out_specs, check_vma=False)
```

```python
import math

import jax
import jax.numpy as jnp
from jax import lax
from jax.experimental import pallas as pl
from jax.experimental.pallas import tpu as pltpu
from jax.sharding import PartitionSpec as P

DH = 128
HEADS = 12
TW = 8


def with_halo(array, sides, width):
    for axis, dim in sides:
        count, length = (lax.axis_size(axis), array.shape[dim])
        up = [(i, (i + 1) % count) for i in range(count - 1)]
        down = [(j, i) for i, j in up]
        last = lax.slice_in_dim(array, length - width, length, axis=dim)
        initial = lax.slice_in_dim(array, 0, width, axis=dim)
        before = lax.ppermute(last, axis, up)
        after = lax.ppermute(initial, axis, down)
        array = jnp.concatenate([before, array, after], axis=dim)
    return array


def window_mask(h, reach_ref, live_ref, own_frames, own_rows, cols, rim_frames, rim_rows):
    own_n = own_frames * own_rows * cols
    rim_n = rim_frames * rim_rows * cols
    own_i = lax.broadcasted_iota(jnp.int32, (own_n, rim_n), 0)
    rim_j = lax.broadcasted_iota(jnp.int32, (own_n, rim_n), 1)
    own_t = own_i // (own_rows * cols)
    own_r = (own_i // cols) % own_rows
    own_c = own_i % cols
    rim_t = rim_j // (rim_rows * cols) - 1
    rim_r = (rim_j // cols) % rim_rows - 1
    rim_c = rim_j % cols
    gap_t = jnp.abs(own_t - rim_t)
    gap_r = jnp.abs(own_r - rim_r)
    gap_w = jnp.abs(own_c // TW - rim_c // TW)
    inside = (
        (gap_t <= reach_ref[0, h])
        & (gap_r <= reach_ref[1, h])
        & (gap_w <= reach_ref[2, h])
    )
    return inside & (live_ref[...] > 0)


def make_query_kernel(dims):
    score_scale = 1.0 / math.sqrt(DH)

    def kernel(reach_ref, q_ref, do_ref, k_ref, v_ref, live_ref, og_ref, lse_ref, dot_ref):
        h = pl.program_id(0)
        window = window_mask(h, reach_ref, live_ref, *dims)
        q_now = q_ref[...]
        do_now = do_ref[...]
        k_rim = k_ref[...]
        v_rim = v_ref[...]
        nt = (((1,), (1,)), ((), ()))
        scores = lax.dot_general(q_now, k_rim, nt, preferred_element_type=jnp.float32) * score_scale
        scores = jnp.where(window, scores, -jnp.inf)
        row_peak = jnp.max(scores, axis=1, keepdims=True)
        log_total = row_peak + jnp.log(jnp.sum(jnp.exp(scores - row_peak), axis=1, keepdims=True))
        weights = jnp.exp(scores - log_total)
        weights_b = weights.astype(jnp.bfloat16)
        out_now = jnp.dot(weights_b, v_rim, preferred_element_type=jnp.float32).astype(jnp.bfloat16)
        row_dot = jnp.sum(
            do_now.astype(jnp.float32) * out_now.astype(jnp.float32), axis=1, keepdims=True
        )
        grad_weights = lax.dot_general(do_now, v_rim, nt, preferred_element_type=jnp.float32)
        grad_scores = (weights * (grad_weights - row_dot)).astype(jnp.bfloat16)
        grad_q = jnp.dot(grad_scores, k_rim, preferred_element_type=jnp.float32) * score_scale
        og_ref[0] = out_now
        og_ref[1] = grad_q.astype(jnp.bfloat16)
        lse_ref[...] = log_total
        dot_ref[...] = row_dot

    return kernel


def make_key_kernel(dims):
    score_scale = 1.0 / math.sqrt(DH)

    def kernel(reach_ref, k_ref, v_ref, q_ref, do_ref, lse_ref, dot_ref, live_ref, gkv_ref):
        h = pl.program_id(0)
        window = window_mask(h, reach_ref, live_ref, *dims)
        k_now = k_ref[...]
        v_now = v_ref[...]
        q_rim = q_ref[...]
        do_rim = do_ref[...]
        nt = (((1,), (1,)), ((), ()))
        scores = lax.dot_general(k_now, q_rim, nt, preferred_element_type=jnp.float32) * score_scale
        scores = jnp.where(window, scores, -jnp.inf)
        weights = jnp.exp(scores - lse_ref[...])
        weights_b = weights.astype(jnp.bfloat16)
        grad_weights = lax.dot_general(v_now, do_rim, nt, preferred_element_type=jnp.float32)
        grad_scores = (weights * (grad_weights - dot_ref[...])).astype(jnp.bfloat16)
        grad_k = jnp.dot(grad_scores, q_rim, preferred_element_type=jnp.float32) * score_scale
        grad_v = jnp.dot(weights_b, do_rim, preferred_element_type=jnp.float32)
        gkv_ref[0] = grad_k.astype(jnp.bfloat16)
        gkv_ref[1] = grad_v.astype(jnp.bfloat16)

    return kernel


def body(queries, key_vectors, value_vectors, out_cotangent, reach_time, reach_height, reach_width):
    lane_count = lax.axis_size("ulysses")
    band_index = lax.axis_index("ulysses")
    time_index = lax.axis_index("tm")
    time_count = lax.axis_size("tm")
    frames_dev, height = queries.shape[0], queries.shape[1]
    rows_dev = height // lane_count
    features = queries.shape[3]
    heads = features // DH
    stacked = jnp.stack([key_vectors, value_vectors, queries, out_cotangent])
    own = lax.all_to_all(stacked, "ulysses", split_axis=2, concat_axis=3, tiled=True)
    col_count = own.shape[3]
    rim_frames, rim_rows = frames_dev + 2, rows_dev + 2
    own_n = frames_dev * rows_dev * col_count
    rim_n = rim_frames * rim_rows * col_count
    own_flat = own.reshape(4, own_n, features)
    kv_rim = with_halo(own[0:2], (("tm", 1), ("ulysses", 2)), 1).reshape(2, rim_n, features)
    qd_rim = with_halo(own[2:4], (("tm", 1), ("ulysses", 2)), 1).reshape(2, rim_n, features)
    dims = (frames_dev, rows_dev, col_count, rim_frames, rim_rows)

    rim_pos = jnp.arange(rim_n, dtype=jnp.int32)
    frame_of = time_index * frames_dev + rim_pos // (rim_rows * col_count) - 1
    row_of = band_index * rows_dev + (rim_pos // col_count) % rim_rows - 1
    live = (
        (frame_of >= 0)
        & (frame_of < time_count * frames_dev)
        & (row_of >= 0)
        & (row_of < height)
    ).astype(jnp.int32).reshape(1, rim_n)
    reach = jnp.stack([reach_time, reach_height, reach_width]).astype(jnp.int32)

    def own_spec(which):
        return pl.BlockSpec((None, own_n, DH), lambda h, r: (which, 0, h))

    def rim_spec(which):
        return pl.BlockSpec((None, rim_n, DH), lambda h, r: (which, 0, h))

    live_spec = pl.BlockSpec((1, rim_n), lambda h, r: (0, 0))
    pair_spec = pl.BlockSpec((2, own_n, DH), lambda h, r: (0, 0, h))
    stat_spec = pl.BlockSpec((None, own_n, 1), lambda h, r: (h, 0, 0))

    og, lse, dots = pl.pallas_call(
        make_query_kernel(dims),
        grid_spec=pltpu.PrefetchScalarGridSpec(
            num_scalar_prefetch=1,
            grid=(heads,),
            in_specs=[own_spec(2), own_spec(3), rim_spec(0), rim_spec(1), live_spec],
            out_specs=[pair_spec, stat_spec, stat_spec],
        ),
        out_shape=[
            jax.ShapeDtypeStruct((2, own_n, features), jnp.bfloat16),
            jax.ShapeDtypeStruct((heads, own_n, 1), jnp.float32),
            jax.ShapeDtypeStruct((heads, own_n, 1), jnp.float32),
        ],
    )(reach, own_flat, own_flat, kv_rim, kv_rim, live)

    def back_to_columns(pair):
        shaped = pair.reshape(2, frames_dev, rows_dev, col_count, features)
        return lax.all_to_all(shaped, "ulysses", split_axis=3, concat_axis=2, tiled=True)

    og_back = back_to_columns(og)

    statistics = jnp.stack([lse, dots]).reshape(2, heads, frames_dev, rows_dev, col_count)
    stat_rim = with_halo(statistics, (("tm", 2), ("ulysses", 3)), 1).reshape(2, heads, 1, rim_n)
    stat_rim_spec = [
        pl.BlockSpec((None, None, 1, rim_n), lambda h, r, w=w: (w, h, 0, 0)) for w in range(2)
    ]
    gkv = pl.pallas_call(
        make_key_kernel(dims),
        grid_spec=pltpu.PrefetchScalarGridSpec(
            num_scalar_prefetch=1,
            grid=(heads,),
            in_specs=[own_spec(0), own_spec(1), rim_spec(0), rim_spec(1)]
            + stat_rim_spec
            + [live_spec],
            out_specs=pair_spec,
        ),
        out_shape=jax.ShapeDtypeStruct((2, own_n, features), jnp.bfloat16),
    )(reach, own_flat, own_flat, qd_rim, qd_rim, stat_rim, stat_rim, live)
    gkv_back = back_to_columns(gkv)
    return (og_back[0], og_back[1], gkv_back[0], gkv_back[1])


def solution(mesh):
    in_specs = (
        P("tm", None, "ulysses", None),
        P("tm", None, "ulysses", None),
        P("tm", None, "ulysses", None),
        P("tm", None, "ulysses", None),
        P(),
        P(),
        P(),
    )
    out_specs = (
        P("tm", None, "ulysses", None),
        P("tm", None, "ulysses", None),
        P("tm", None, "ulysses", None),
        P("tm", None, "ulysses", None),
    )
    return jax.shard_map(body, mesh=mesh, in_specs=in_specs, out_specs=out_specs, check_vma=False)
```

```python
import math

import jax
import jax.numpy as jnp
from jax import lax
from jax.experimental import pallas as pl
from jax.experimental.pallas import tpu as pltpu
from jax.sharding import Mesh, PartitionSpec as P

DH = 128
HEADS = 12
TW = 8


def with_halo(array, sides, width):
    for axis, dim in sides:
        count, length = (lax.axis_size(axis), array.shape[dim])
        up = [(i, (i + 1) % count) for i in range(count - 1)]
        down = [(j, i) for i, j in up]
        last = lax.slice_in_dim(array, length - width, length, axis=dim)
        initial = lax.slice_in_dim(array, 0, width, axis=dim)
        before = lax.ppermute(last, axis, up)
        after = lax.ppermute(initial, axis, down)
        array = jnp.concatenate([before, array, after], axis=dim)
    return array


def window_mask(h, reach_ref, live_ref, own_frames, own_rows, cols, rim_frames, rim_rows):
    own_n = own_frames * own_rows * cols
    rim_n = rim_frames * rim_rows * cols
    own_i = lax.broadcasted_iota(jnp.int32, (own_n, rim_n), 0)
    rim_j = lax.broadcasted_iota(jnp.int32, (own_n, rim_n), 1)
    own_t = own_i // (own_rows * cols)
    own_r = (own_i // cols) % own_rows
    own_c = own_i % cols
    rim_t = rim_j // (rim_rows * cols) - 1
    rim_r = (rim_j // cols) % rim_rows - 1
    rim_c = rim_j % cols
    gap_t = jnp.abs(own_t - rim_t)
    gap_r = jnp.abs(own_r - rim_r)
    gap_w = jnp.abs(own_c // TW - rim_c // TW)
    inside = (
        (gap_t <= reach_ref[0, h])
        & (gap_r <= reach_ref[1, h])
        & (gap_w <= reach_ref[2, h])
    )
    return inside & (live_ref[...] > 0)


def make_query_kernel(dims):
    score_scale = 1.0 / math.sqrt(DH)

    def kernel(reach_ref, q_ref, do_ref, k_ref, v_ref, live_ref, og_ref, lse_ref, dot_ref):
        h = pl.program_id(0)
        window = window_mask(h, reach_ref, live_ref, *dims)
        q_now = q_ref[...]
        do_now = do_ref[...]
        k_rim = k_ref[...]
        v_rim = v_ref[...]
        nt = (((1,), (1,)), ((), ()))
        scores = lax.dot_general(q_now, k_rim, nt, preferred_element_type=jnp.float32) * score_scale
        scores = jnp.where(window, scores, -jnp.inf)
        row_peak = jnp.max(scores, axis=1, keepdims=True)
        log_total = row_peak + jnp.log(jnp.sum(jnp.exp(scores - row_peak), axis=1, keepdims=True))
        weights = jnp.exp(scores - log_total)
        weights_b = weights.astype(jnp.bfloat16)
        out_now = jnp.dot(weights_b, v_rim, preferred_element_type=jnp.float32).astype(jnp.bfloat16)
        row_dot = jnp.sum(
            do_now.astype(jnp.float32) * out_now.astype(jnp.float32), axis=1, keepdims=True
        )
        grad_weights = lax.dot_general(do_now, v_rim, nt, preferred_element_type=jnp.float32)
        grad_scores = (weights * (grad_weights - row_dot)).astype(jnp.bfloat16)
        grad_q = jnp.dot(grad_scores, k_rim, preferred_element_type=jnp.float32) * score_scale
        og_ref[0] = out_now
        og_ref[1] = grad_q.astype(jnp.bfloat16)
        lse_ref[...] = log_total
        dot_ref[...] = row_dot

    return kernel


def make_key_kernel(dims):
    score_scale = 1.0 / math.sqrt(DH)

    def kernel(reach_ref, k_ref, v_ref, q_ref, do_ref, lse_ref, dot_ref, live_ref, gkv_ref):
        h = pl.program_id(0)
        window = window_mask(h, reach_ref, live_ref, *dims)
        k_now = k_ref[...]
        v_now = v_ref[...]
        q_rim = q_ref[...]
        do_rim = do_ref[...]
        nt = (((1,), (1,)), ((), ()))
        scores = lax.dot_general(k_now, q_rim, nt, preferred_element_type=jnp.float32) * score_scale
        scores = jnp.where(window, scores, -jnp.inf)
        weights = jnp.exp(scores - lse_ref[...])
        weights_b = weights.astype(jnp.bfloat16)
        grad_weights = lax.dot_general(v_now, do_rim, nt, preferred_element_type=jnp.float32)
        grad_scores = (weights * (grad_weights - dot_ref[...])).astype(jnp.bfloat16)
        grad_k = jnp.dot(grad_scores, q_rim, preferred_element_type=jnp.float32) * score_scale
        grad_v = jnp.dot(weights_b, do_rim, preferred_element_type=jnp.float32)
        gkv_ref[0] = grad_k.astype(jnp.bfloat16)
        gkv_ref[1] = grad_v.astype(jnp.bfloat16)

    return kernel


def body(queries, key_vectors, value_vectors, out_cotangent, reach_time, reach_height, reach_width):
    lane_count = lax.axis_size(("z", "core"))
    band_index = lax.axis_index(("z", "core"))
    time_index = lax.axis_index("tm")
    time_count = lax.axis_size("tm")
    frames_dev, height = queries.shape[0], queries.shape[1]
    rows_dev = height // lane_count
    features = queries.shape[3]
    heads = features // DH
    stacked = jnp.stack([key_vectors, value_vectors, queries, out_cotangent])
    chips, cores = lax.axis_size("z"), lax.axis_size("core")
    local_cols = stacked.shape[3]
    across = lax.all_to_all(stacked, "z", split_axis=2, concat_axis=3, tiled=True)
    across = across.reshape(across.shape[:3] + (chips, 1, local_cols, features))
    own = lax.all_to_all(across, "core", split_axis=2, concat_axis=4, tiled=True)
    own = own.reshape(own.shape[:3] + (-1, features))
    col_count = own.shape[3]
    rim_frames, rim_rows = frames_dev + 2, rows_dev + 2
    own_n = frames_dev * rows_dev * col_count
    rim_n = rim_frames * rim_rows * col_count
    own_flat = own.reshape(4, own_n, features)
    kv_rim = with_halo(own[0:2], (("tm", 1), (("z", "core"), 2)), 1).reshape(2, rim_n, features)
    qd_rim = with_halo(own[2:4], (("tm", 1), (("z", "core"), 2)), 1).reshape(2, rim_n, features)
    dims = (frames_dev, rows_dev, col_count, rim_frames, rim_rows)

    rim_pos = jnp.arange(rim_n, dtype=jnp.int32)
    frame_of = time_index * frames_dev + rim_pos // (rim_rows * col_count) - 1
    row_of = band_index * rows_dev + (rim_pos // col_count) % rim_rows - 1
    live = (
        (frame_of >= 0)
        & (frame_of < time_count * frames_dev)
        & (row_of >= 0)
        & (row_of < height)
    ).astype(jnp.int32).reshape(1, rim_n)
    reach = jnp.stack([reach_time, reach_height, reach_width]).astype(jnp.int32)

    def own_spec(which):
        return pl.BlockSpec((None, own_n, DH), lambda h, r: (which, 0, h))

    def rim_spec(which):
        return pl.BlockSpec((None, rim_n, DH), lambda h, r: (which, 0, h))

    live_spec = pl.BlockSpec((1, rim_n), lambda h, r: (0, 0))
    pair_spec = pl.BlockSpec((2, own_n, DH), lambda h, r: (0, 0, h))
    stat_spec = pl.BlockSpec((None, own_n, 1), lambda h, r: (h, 0, 0))

    og, lse, dots = pl.pallas_call(
        make_query_kernel(dims),
        grid_spec=pltpu.PrefetchScalarGridSpec(
            num_scalar_prefetch=1,
            grid=(heads,),
            in_specs=[own_spec(2), own_spec(3), rim_spec(0), rim_spec(1), live_spec],
            out_specs=[pair_spec, stat_spec, stat_spec],
        ),
        out_shape=[
            jax.ShapeDtypeStruct((2, own_n, features), jnp.bfloat16),
            jax.ShapeDtypeStruct((heads, own_n, 1), jnp.float32),
            jax.ShapeDtypeStruct((heads, own_n, 1), jnp.float32),
        ],
    )(reach, own_flat, own_flat, kv_rim, kv_rim, live)

    def back_to_columns(pair):
        shaped = pair.reshape(2, frames_dev, rows_dev, chips, cores, local_cols, features)
        within = lax.all_to_all(shaped, "core", split_axis=4, concat_axis=2, tiled=True)
        within = within.reshape(2, frames_dev, rows_dev * cores, chips * local_cols, features)
        return lax.all_to_all(within, "z", split_axis=3, concat_axis=2, tiled=True)

    og_back = back_to_columns(og)

    statistics = jnp.stack([lse, dots]).reshape(2, heads, frames_dev, rows_dev, col_count)
    stat_rim = with_halo(statistics, (("tm", 2), (("z", "core"), 3)), 1).reshape(2, heads, 1, rim_n)
    stat_rim_spec = [
        pl.BlockSpec((None, None, 1, rim_n), lambda h, r, w=w: (w, h, 0, 0)) for w in range(2)
    ]
    gkv = pl.pallas_call(
        make_key_kernel(dims),
        grid_spec=pltpu.PrefetchScalarGridSpec(
            num_scalar_prefetch=1,
            grid=(heads,),
            in_specs=[own_spec(0), own_spec(1), rim_spec(0), rim_spec(1)]
            + stat_rim_spec
            + [live_spec],
            out_specs=pair_spec,
        ),
        out_shape=jax.ShapeDtypeStruct((2, own_n, features), jnp.bfloat16),
    )(reach, own_flat, own_flat, qd_rim, qd_rim, stat_rim, stat_rim, live)
    gkv_back = back_to_columns(gkv)
    return (og_back[0], og_back[1], gkv_back[0], gkv_back[1])


def solution(mesh):
    in_specs = (
        P("tm", None, ("z", "core"), None),
        P("tm", None, ("z", "core"), None),
        P("tm", None, ("z", "core"), None),
        P("tm", None, ("z", "core"), None),
        P(),
        P(),
        P(),
    )
    out_specs = (
        P("tm", None, ("z", "core"), None),
        P("tm", None, ("z", "core"), None),
        P("tm", None, ("z", "core"), None),
        P("tm", None, ("z", "core"), None),
    )
    tm_size, lane_size = mesh.shape["tm"], mesh.shape["ulysses"]
    cores = 2 if lane_size % 2 == 0 else 1
    split = Mesh(mesh.devices.reshape(tm_size, lane_size // cores, cores), ("tm", "z", "core"))
    return jax.shard_map(body, mesh=split, in_specs=in_specs, out_specs=out_specs, check_vma=False)
```

```python
import math

import jax
import jax.numpy as jnp
from jax import lax
from jax.experimental import pallas as pl
from jax.experimental.pallas import tpu as pltpu
from jax.sharding import PartitionSpec as P

DH = 128
HEADS = 12
TW = 8


def with_halo(array, sides, width):
    for axis, dim in sides:
        count, length = (lax.axis_size(axis), array.shape[dim])
        up = [(i, (i + 1) % count) for i in range(count - 1)]
        down = [(j, i) for i, j in up]
        last = lax.slice_in_dim(array, length - width, length, axis=dim)
        initial = lax.slice_in_dim(array, 0, width, axis=dim)
        before = lax.ppermute(last, axis, up)
        after = lax.ppermute(initial, axis, down)
        array = jnp.concatenate([before, array, after], axis=dim)
    return array


def window_mask(h, reach_ref, gap_ref):
    return (
        (gap_ref[0] <= reach_ref[0, h])
        & (gap_ref[1] <= reach_ref[1, h])
        & (gap_ref[2] <= reach_ref[2, h])
    )


def gap_table(live, own_frames, own_rows, cols, rim_frames, rim_rows):
    own_n = own_frames * own_rows * cols
    rim_n = rim_frames * rim_rows * cols
    own_i = jnp.arange(own_n, dtype=jnp.int32)[:, None]
    rim_j = jnp.arange(rim_n, dtype=jnp.int32)[None, :]
    own_t = own_i // (own_rows * cols)
    own_r = (own_i // cols) % own_rows
    own_c = own_i % cols
    rim_t = rim_j // (rim_rows * cols) - 1
    rim_r = (rim_j // cols) % rim_rows - 1
    rim_c = rim_j % cols
    gap_t = jnp.where(live, jnp.abs(own_t - rim_t), own_n + rim_n)
    gap_r = jnp.abs(own_r - rim_r)
    gap_w = jnp.abs(own_c // TW - rim_c // TW)
    return jnp.stack(jnp.broadcast_arrays(gap_t, gap_r, gap_w)).astype(jnp.int32)


def make_query_kernel():
    score_scale = 1.0 / math.sqrt(DH)

    def kernel(reach_ref, q_ref, do_ref, k_ref, v_ref, gap_ref, og_ref, lse_ref, dot_ref):
        h = pl.program_id(0)
        window = window_mask(h, reach_ref, gap_ref)
        q_now = q_ref[...]
        do_now = do_ref[...]
        k_rim = k_ref[...]
        v_rim = v_ref[...]
        nt = (((1,), (1,)), ((), ()))
        scores = lax.dot_general(q_now, k_rim, nt, preferred_element_type=jnp.float32) * score_scale
        scores = jnp.where(window, scores, -jnp.inf)
        row_peak = jnp.max(scores, axis=1, keepdims=True)
        log_total = row_peak + jnp.log(jnp.sum(jnp.exp(scores - row_peak), axis=1, keepdims=True))
        weights = jnp.exp(scores - log_total)
        weights_b = weights.astype(jnp.bfloat16)
        out_now = jnp.dot(weights_b, v_rim, preferred_element_type=jnp.float32).astype(jnp.bfloat16)
        row_dot = jnp.sum(
            do_now.astype(jnp.float32) * out_now.astype(jnp.float32), axis=1, keepdims=True
        )
        grad_weights = lax.dot_general(do_now, v_rim, nt, preferred_element_type=jnp.float32)
        grad_scores = (weights * (grad_weights - row_dot)).astype(jnp.bfloat16)
        grad_q = jnp.dot(grad_scores, k_rim, preferred_element_type=jnp.float32) * score_scale
        og_ref[0] = out_now
        og_ref[1] = grad_q.astype(jnp.bfloat16)
        lse_ref[...] = log_total
        dot_ref[...] = row_dot

    return kernel


def make_key_kernel():
    score_scale = 1.0 / math.sqrt(DH)

    def kernel(reach_ref, k_ref, v_ref, q_ref, do_ref, lse_ref, dot_ref, gap_ref, gkv_ref):
        h = pl.program_id(0)
        window = window_mask(h, reach_ref, gap_ref)
        k_now = k_ref[...]
        v_now = v_ref[...]
        q_rim = q_ref[...]
        do_rim = do_ref[...]
        nt = (((1,), (1,)), ((), ()))
        scores = lax.dot_general(k_now, q_rim, nt, preferred_element_type=jnp.float32) * score_scale
        scores = jnp.where(window, scores, -jnp.inf)
        weights = jnp.exp(scores - lse_ref[...])
        weights_b = weights.astype(jnp.bfloat16)
        grad_weights = lax.dot_general(v_now, do_rim, nt, preferred_element_type=jnp.float32)
        grad_scores = (weights * (grad_weights - dot_ref[...])).astype(jnp.bfloat16)
        grad_k = jnp.dot(grad_scores, q_rim, preferred_element_type=jnp.float32) * score_scale
        grad_v = jnp.dot(weights_b, do_rim, preferred_element_type=jnp.float32)
        gkv_ref[0] = grad_k.astype(jnp.bfloat16)
        gkv_ref[1] = grad_v.astype(jnp.bfloat16)

    return kernel


def body(queries, key_vectors, value_vectors, out_cotangent, reach_time, reach_height, reach_width):
    lane_count = lax.axis_size("ulysses")
    band_index = lax.axis_index("ulysses")
    time_index = lax.axis_index("tm")
    time_count = lax.axis_size("tm")
    frames_dev, height = queries.shape[0], queries.shape[1]
    rows_dev = height // lane_count
    features = queries.shape[3]
    heads = features // DH
    stacked = jnp.stack([key_vectors, value_vectors, queries, out_cotangent])
    own = lax.all_to_all(stacked, "ulysses", split_axis=2, concat_axis=3, tiled=True)
    col_count = own.shape[3]
    rim_frames, rim_rows = frames_dev + 2, rows_dev + 2
    own_n = frames_dev * rows_dev * col_count
    rim_n = rim_frames * rim_rows * col_count
    own_flat = own.reshape(4, own_n, features)
    kv_rim = with_halo(own[0:2], (("tm", 1), ("ulysses", 2)), 1).reshape(2, rim_n, features)
    qd_rim = with_halo(own[2:4], (("tm", 1), ("ulysses", 2)), 1).reshape(2, rim_n, features)
    dims = (frames_dev, rows_dev, col_count, rim_frames, rim_rows)

    rim_pos = jnp.arange(rim_n, dtype=jnp.int32)
    frame_of = time_index * frames_dev + rim_pos // (rim_rows * col_count) - 1
    row_of = band_index * rows_dev + (rim_pos // col_count) % rim_rows - 1
    live = (
        (frame_of >= 0)
        & (frame_of < time_count * frames_dev)
        & (row_of >= 0)
        & (row_of < height)
    ).reshape(1, rim_n)
    gaps = gap_table(live, *dims)
    reach = jnp.stack([reach_time, reach_height, reach_width]).astype(jnp.int32)

    def own_spec(which):
        return pl.BlockSpec((None, own_n, DH), lambda h, r: (which, 0, h))

    def rim_spec(which):
        return pl.BlockSpec((None, rim_n, DH), lambda h, r: (which, 0, h))

    live_spec = pl.BlockSpec((3, own_n, rim_n), lambda h, r: (0, 0, 0))
    pair_spec = pl.BlockSpec((2, own_n, DH), lambda h, r: (0, 0, h))
    stat_spec = pl.BlockSpec((None, own_n, 1), lambda h, r: (h, 0, 0))

    og, lse, dots = pl.pallas_call(
        make_query_kernel(),
        grid_spec=pltpu.PrefetchScalarGridSpec(
            num_scalar_prefetch=1,
            grid=(heads,),
            in_specs=[own_spec(2), own_spec(3), rim_spec(0), rim_spec(1), live_spec],
            out_specs=[pair_spec, stat_spec, stat_spec],
        ),
        out_shape=[
            jax.ShapeDtypeStruct((2, own_n, features), jnp.bfloat16),
            jax.ShapeDtypeStruct((heads, own_n, 1), jnp.float32),
            jax.ShapeDtypeStruct((heads, own_n, 1), jnp.float32),
        ],
    )(reach, own_flat, own_flat, kv_rim, kv_rim, gaps)

    def back_to_columns(pair):
        shaped = pair.reshape(2, frames_dev, rows_dev, col_count, features)
        return lax.all_to_all(shaped, "ulysses", split_axis=3, concat_axis=2, tiled=True)

    og_back = back_to_columns(og)

    statistics = jnp.stack([lse, dots]).reshape(2, heads, frames_dev, rows_dev, col_count)
    stat_rim = with_halo(statistics, (("tm", 2), ("ulysses", 3)), 1).reshape(2, heads, 1, rim_n)
    stat_rim_spec = [
        pl.BlockSpec((None, None, 1, rim_n), lambda h, r, w=w: (w, h, 0, 0)) for w in range(2)
    ]
    gkv = pl.pallas_call(
        make_key_kernel(),
        grid_spec=pltpu.PrefetchScalarGridSpec(
            num_scalar_prefetch=1,
            grid=(heads,),
            in_specs=[own_spec(0), own_spec(1), rim_spec(0), rim_spec(1)]
            + stat_rim_spec
            + [live_spec],
            out_specs=pair_spec,
        ),
        out_shape=jax.ShapeDtypeStruct((2, own_n, features), jnp.bfloat16),
    )(reach, own_flat, own_flat, qd_rim, qd_rim, stat_rim, stat_rim, gaps)
    gkv_back = back_to_columns(gkv)
    return (og_back[0], og_back[1], gkv_back[0], gkv_back[1])


def solution(mesh):
    in_specs = (
        P("tm", None, "ulysses", None),
        P("tm", None, "ulysses", None),
        P("tm", None, "ulysses", None),
        P("tm", None, "ulysses", None),
        P(),
        P(),
        P(),
    )
    out_specs = (
        P("tm", None, "ulysses", None),
        P("tm", None, "ulysses", None),
        P("tm", None, "ulysses", None),
        P("tm", None, "ulysses", None),
    )
    return jax.shard_map(body, mesh=mesh, in_specs=in_specs, out_specs=out_specs, check_vma=False)
```

```python
import math

import jax
import jax.numpy as jnp
from jax import lax
from jax.experimental import pallas as pl
from jax.experimental.pallas import tpu as pltpu
from jax.sharding import PartitionSpec as P

DH = 128
HEADS = 12
TW = 8
PER_STEP = 2


def with_halo(array, sides, width):
    for axis, dim in sides:
        count, length = (lax.axis_size(axis), array.shape[dim])
        up = [(i, (i + 1) % count) for i in range(count - 1)]
        down = [(j, i) for i, j in up]
        last = lax.slice_in_dim(array, length - width, length, axis=dim)
        initial = lax.slice_in_dim(array, 0, width, axis=dim)
        before = lax.ppermute(last, axis, up)
        after = lax.ppermute(initial, axis, down)
        array = jnp.concatenate([before, array, after], axis=dim)
    return array


def window_mask(h, reach_ref, gap_ref):
    return (
        (gap_ref[0] <= reach_ref[0, h])
        & (gap_ref[1] <= reach_ref[1, h])
        & (gap_ref[2] <= reach_ref[2, h])
    )


def gap_table(live, own_frames, own_rows, cols, rim_frames, rim_rows):
    own_n = own_frames * own_rows * cols
    rim_n = rim_frames * rim_rows * cols
    own_i = jnp.arange(own_n, dtype=jnp.int32)[:, None]
    rim_j = jnp.arange(rim_n, dtype=jnp.int32)[None, :]
    own_t = own_i // (own_rows * cols)
    own_r = (own_i // cols) % own_rows
    own_c = own_i % cols
    rim_t = rim_j // (rim_rows * cols) - 1
    rim_r = (rim_j // cols) % rim_rows - 1
    rim_c = rim_j % cols
    gap_t = jnp.where(live, jnp.abs(own_t - rim_t), own_n + rim_n)
    gap_r = jnp.abs(own_r - rim_r)
    gap_w = jnp.abs(own_c // TW - rim_c // TW)
    return jnp.stack(jnp.broadcast_arrays(gap_t, gap_r, gap_w)).astype(jnp.int32)


def make_query_kernel():
    score_scale = 1.0 / math.sqrt(DH)

    def kernel(reach_ref, q_ref, do_ref, k_ref, v_ref, gap_ref, og_ref, lse_ref, dot_ref):
      for j in range(PER_STEP):
        lanes = pl.ds(j * DH, DH)
        window = window_mask(pl.program_id(0) * PER_STEP + j, reach_ref, gap_ref)
        q_now = q_ref[:, lanes]
        do_now = do_ref[:, lanes]
        k_rim = k_ref[:, lanes]
        v_rim = v_ref[:, lanes]
        nt = (((1,), (1,)), ((), ()))
        scores = lax.dot_general(q_now, k_rim, nt, preferred_element_type=jnp.float32) * score_scale
        scores = jnp.where(window, scores, -jnp.inf)
        row_peak = jnp.max(scores, axis=1, keepdims=True)
        log_total = row_peak + jnp.log(jnp.sum(jnp.exp(scores - row_peak), axis=1, keepdims=True))
        weights = jnp.exp(scores - log_total)
        weights_b = weights.astype(jnp.bfloat16)
        out_now = jnp.dot(weights_b, v_rim, preferred_element_type=jnp.float32).astype(jnp.bfloat16)
        row_dot = jnp.sum(
            do_now.astype(jnp.float32) * out_now.astype(jnp.float32), axis=1, keepdims=True
        )
        grad_weights = lax.dot_general(do_now, v_rim, nt, preferred_element_type=jnp.float32)
        grad_scores = (weights * (grad_weights - row_dot)).astype(jnp.bfloat16)
        grad_q = jnp.dot(grad_scores, k_rim, preferred_element_type=jnp.float32) * score_scale
        og_ref[0, :, lanes] = out_now
        og_ref[1, :, lanes] = grad_q.astype(jnp.bfloat16)
        lse_ref[j] = log_total
        dot_ref[j] = row_dot

    return kernel


def make_key_kernel():
    score_scale = 1.0 / math.sqrt(DH)

    def kernel(reach_ref, k_ref, v_ref, q_ref, do_ref, lse_ref, dot_ref, gap_ref, gkv_ref):
      for j in range(PER_STEP):
        lanes = pl.ds(j * DH, DH)
        window = window_mask(pl.program_id(0) * PER_STEP + j, reach_ref, gap_ref)
        k_now = k_ref[:, lanes]
        v_now = v_ref[:, lanes]
        q_rim = q_ref[:, lanes]
        do_rim = do_ref[:, lanes]
        nt = (((1,), (1,)), ((), ()))
        scores = lax.dot_general(k_now, q_rim, nt, preferred_element_type=jnp.float32) * score_scale
        scores = jnp.where(window, scores, -jnp.inf)
        weights = jnp.exp(scores - lse_ref[j])
        weights_b = weights.astype(jnp.bfloat16)
        grad_weights = lax.dot_general(v_now, do_rim, nt, preferred_element_type=jnp.float32)
        grad_scores = (weights * (grad_weights - dot_ref[j])).astype(jnp.bfloat16)
        grad_k = jnp.dot(grad_scores, q_rim, preferred_element_type=jnp.float32) * score_scale
        grad_v = jnp.dot(weights_b, do_rim, preferred_element_type=jnp.float32)
        gkv_ref[0, :, lanes] = grad_k.astype(jnp.bfloat16)
        gkv_ref[1, :, lanes] = grad_v.astype(jnp.bfloat16)

    return kernel


def body(queries, key_vectors, value_vectors, out_cotangent, reach_time, reach_height, reach_width):
    lane_count = lax.axis_size("ulysses")
    band_index = lax.axis_index("ulysses")
    time_index = lax.axis_index("tm")
    time_count = lax.axis_size("tm")
    frames_dev, height = queries.shape[0], queries.shape[1]
    rows_dev = height // lane_count
    features = queries.shape[3]
    heads = features // DH
    stacked = jnp.stack([key_vectors, value_vectors, queries, out_cotangent])
    own = lax.all_to_all(stacked, "ulysses", split_axis=2, concat_axis=3, tiled=True)
    col_count = own.shape[3]
    rim_frames, rim_rows = frames_dev + 2, rows_dev + 2
    own_n = frames_dev * rows_dev * col_count
    rim_n = rim_frames * rim_rows * col_count
    own_flat = own.reshape(4, own_n, features)
    kv_rim = with_halo(own[0:2], (("tm", 1), ("ulysses", 2)), 1).reshape(2, rim_n, features)
    qd_rim = with_halo(own[2:4], (("tm", 1), ("ulysses", 2)), 1).reshape(2, rim_n, features)
    dims = (frames_dev, rows_dev, col_count, rim_frames, rim_rows)

    rim_pos = jnp.arange(rim_n, dtype=jnp.int32)
    frame_of = time_index * frames_dev + rim_pos // (rim_rows * col_count) - 1
    row_of = band_index * rows_dev + (rim_pos // col_count) % rim_rows - 1
    live = (
        (frame_of >= 0)
        & (frame_of < time_count * frames_dev)
        & (row_of >= 0)
        & (row_of < height)
    ).reshape(1, rim_n)
    gaps = gap_table(live, *dims)
    reach = jnp.stack([reach_time, reach_height, reach_width]).astype(jnp.int32)

    def own_spec(which):
        return pl.BlockSpec((None, own_n, DH * PER_STEP), lambda h, r: (which, 0, h))

    def rim_spec(which):
        return pl.BlockSpec((None, rim_n, DH * PER_STEP), lambda h, r: (which, 0, h))

    live_spec = pl.BlockSpec((3, own_n, rim_n), lambda h, r: (0, 0, 0))
    pair_spec = pl.BlockSpec((2, own_n, DH * PER_STEP), lambda h, r: (0, 0, h))
    stat_spec = pl.BlockSpec((PER_STEP, own_n, 1), lambda h, r: (h, 0, 0))

    og, lse, dots = pl.pallas_call(
        make_query_kernel(),
        grid_spec=pltpu.PrefetchScalarGridSpec(
            num_scalar_prefetch=1,
            grid=(heads // PER_STEP,),
            in_specs=[own_spec(2), own_spec(3), rim_spec(0), rim_spec(1), live_spec],
            out_specs=[pair_spec, stat_spec, stat_spec],
        ),
        out_shape=[
            jax.ShapeDtypeStruct((2, own_n, features), jnp.bfloat16),
            jax.ShapeDtypeStruct((heads, own_n, 1), jnp.float32),
            jax.ShapeDtypeStruct((heads, own_n, 1), jnp.float32),
        ],
    )(reach, own_flat, own_flat, kv_rim, kv_rim, gaps)

    def back_to_columns(pair):
        shaped = pair.reshape(2, frames_dev, rows_dev, col_count, features)
        return lax.all_to_all(shaped, "ulysses", split_axis=3, concat_axis=2, tiled=True)

    og_back = back_to_columns(og)

    statistics = jnp.stack([lse, dots]).reshape(2, heads, frames_dev, rows_dev, col_count)
    stat_rim = with_halo(statistics, (("tm", 2), ("ulysses", 3)), 1).reshape(2, heads, 1, rim_n)
    stat_rim_spec = [
        pl.BlockSpec((None, PER_STEP, 1, rim_n), lambda h, r, w=w: (w, h, 0, 0)) for w in range(2)
    ]
    gkv = pl.pallas_call(
        make_key_kernel(),
        grid_spec=pltpu.PrefetchScalarGridSpec(
            num_scalar_prefetch=1,
            grid=(heads // PER_STEP,),
            in_specs=[own_spec(0), own_spec(1), rim_spec(0), rim_spec(1)]
            + stat_rim_spec
            + [live_spec],
            out_specs=pair_spec,
        ),
        out_shape=jax.ShapeDtypeStruct((2, own_n, features), jnp.bfloat16),
    )(reach, own_flat, own_flat, qd_rim, qd_rim, stat_rim, stat_rim, gaps)
    gkv_back = back_to_columns(gkv)
    return (og_back[0], og_back[1], gkv_back[0], gkv_back[1])


def solution(mesh):
    in_specs = (
        P("tm", None, "ulysses", None),
        P("tm", None, "ulysses", None),
        P("tm", None, "ulysses", None),
        P("tm", None, "ulysses", None),
        P(),
        P(),
        P(),
    )
    out_specs = (
        P("tm", None, "ulysses", None),
        P("tm", None, "ulysses", None),
        P("tm", None, "ulysses", None),
        P("tm", None, "ulysses", None),
    )
    return jax.shard_map(body, mesh=mesh, in_specs=in_specs, out_specs=out_specs, check_vma=False)
```

```python
import math

import jax
import jax.numpy as jnp
from jax import lax
from jax.experimental import pallas as pl
from jax.experimental.pallas import tpu as pltpu
from jax.sharding import PartitionSpec as P

DH = 128
HEADS = 12
TW = 8
PER_STEP = 4


def with_halo(array, sides, width):
    for axis, dim in sides:
        count, length = (lax.axis_size(axis), array.shape[dim])
        up = [(i, (i + 1) % count) for i in range(count - 1)]
        down = [(j, i) for i, j in up]
        last = lax.slice_in_dim(array, length - width, length, axis=dim)
        initial = lax.slice_in_dim(array, 0, width, axis=dim)
        before = lax.ppermute(last, axis, up)
        after = lax.ppermute(initial, axis, down)
        array = jnp.concatenate([before, array, after], axis=dim)
    return array


def window_mask(h, reach_ref, gap_ref):
    return (
        (gap_ref[0] <= reach_ref[0, h])
        & (gap_ref[1] <= reach_ref[1, h])
        & (gap_ref[2] <= reach_ref[2, h])
    )


def gap_table(live, own_frames, own_rows, cols, rim_frames, rim_rows):
    own_n = own_frames * own_rows * cols
    rim_n = rim_frames * rim_rows * cols
    own_i = jnp.arange(own_n, dtype=jnp.int32)[:, None]
    rim_j = jnp.arange(rim_n, dtype=jnp.int32)[None, :]
    own_t = own_i // (own_rows * cols)
    own_r = (own_i // cols) % own_rows
    own_c = own_i % cols
    rim_t = rim_j // (rim_rows * cols) - 1
    rim_r = (rim_j // cols) % rim_rows - 1
    rim_c = rim_j % cols
    gap_t = jnp.where(live, jnp.abs(own_t - rim_t), own_n + rim_n)
    gap_r = jnp.abs(own_r - rim_r)
    gap_w = jnp.abs(own_c // TW - rim_c // TW)
    return jnp.stack(jnp.broadcast_arrays(gap_t, gap_r, gap_w)).astype(jnp.int32)


def make_query_kernel():
    score_scale = 1.0 / math.sqrt(DH)

    def kernel(reach_ref, q_ref, do_ref, k_ref, v_ref, gap_ref, og_ref, lse_ref, dot_ref):
      for j in range(PER_STEP):
        lanes = pl.ds(j * DH, DH)
        window = window_mask(pl.program_id(0) * PER_STEP + j, reach_ref, gap_ref)
        q_now = q_ref[:, lanes]
        do_now = do_ref[:, lanes]
        k_rim = k_ref[:, lanes]
        v_rim = v_ref[:, lanes]
        nt = (((1,), (1,)), ((), ()))
        scores = lax.dot_general(q_now, k_rim, nt, preferred_element_type=jnp.float32) * score_scale
        scores = jnp.where(window, scores, -jnp.inf)
        row_peak = jnp.max(scores, axis=1, keepdims=True)
        log_total = row_peak + jnp.log(jnp.sum(jnp.exp(scores - row_peak), axis=1, keepdims=True))
        weights = jnp.exp(scores - log_total)
        weights_b = weights.astype(jnp.bfloat16)
        out_now = jnp.dot(weights_b, v_rim, preferred_element_type=jnp.float32).astype(jnp.bfloat16)
        row_dot = jnp.sum(
            do_now.astype(jnp.float32) * out_now.astype(jnp.float32), axis=1, keepdims=True
        )
        grad_weights = lax.dot_general(do_now, v_rim, nt, preferred_element_type=jnp.float32)
        grad_scores = (weights * (grad_weights - row_dot)).astype(jnp.bfloat16)
        grad_q = jnp.dot(grad_scores, k_rim, preferred_element_type=jnp.float32) * score_scale
        og_ref[0, :, lanes] = out_now
        og_ref[1, :, lanes] = grad_q.astype(jnp.bfloat16)
        lse_ref[j] = log_total
        dot_ref[j] = row_dot

    return kernel


def make_key_kernel():
    score_scale = 1.0 / math.sqrt(DH)

    def kernel(reach_ref, k_ref, v_ref, q_ref, do_ref, lse_ref, dot_ref, gap_ref, gkv_ref):
      for j in range(PER_STEP):
        lanes = pl.ds(j * DH, DH)
        window = window_mask(pl.program_id(0) * PER_STEP + j, reach_ref, gap_ref)
        k_now = k_ref[:, lanes]
        v_now = v_ref[:, lanes]
        q_rim = q_ref[:, lanes]
        do_rim = do_ref[:, lanes]
        nt = (((1,), (1,)), ((), ()))
        scores = lax.dot_general(k_now, q_rim, nt, preferred_element_type=jnp.float32) * score_scale
        scores = jnp.where(window, scores, -jnp.inf)
        weights = jnp.exp(scores - lse_ref[j])
        weights_b = weights.astype(jnp.bfloat16)
        grad_weights = lax.dot_general(v_now, do_rim, nt, preferred_element_type=jnp.float32)
        grad_scores = (weights * (grad_weights - dot_ref[j])).astype(jnp.bfloat16)
        grad_k = jnp.dot(grad_scores, q_rim, preferred_element_type=jnp.float32) * score_scale
        grad_v = jnp.dot(weights_b, do_rim, preferred_element_type=jnp.float32)
        gkv_ref[0, :, lanes] = grad_k.astype(jnp.bfloat16)
        gkv_ref[1, :, lanes] = grad_v.astype(jnp.bfloat16)

    return kernel


def body(queries, key_vectors, value_vectors, out_cotangent, reach_time, reach_height, reach_width):
    lane_count = lax.axis_size("ulysses")
    band_index = lax.axis_index("ulysses")
    time_index = lax.axis_index("tm")
    time_count = lax.axis_size("tm")
    frames_dev, height = queries.shape[0], queries.shape[1]
    rows_dev = height // lane_count
    features = queries.shape[3]
    heads = features // DH
    stacked = jnp.stack([key_vectors, value_vectors, queries, out_cotangent])
    own = lax.all_to_all(stacked, "ulysses", split_axis=2, concat_axis=3, tiled=True)
    col_count = own.shape[3]
    rim_frames, rim_rows = frames_dev + 2, rows_dev + 2
    own_n = frames_dev * rows_dev * col_count
    rim_n = rim_frames * rim_rows * col_count
    own_flat = own.reshape(4, own_n, features)
    kv_rim = with_halo(own[0:2], (("tm", 1), ("ulysses", 2)), 1).reshape(2, rim_n, features)
    qd_rim = with_halo(own[2:4], (("tm", 1), ("ulysses", 2)), 1).reshape(2, rim_n, features)
    dims = (frames_dev, rows_dev, col_count, rim_frames, rim_rows)

    rim_pos = jnp.arange(rim_n, dtype=jnp.int32)
    frame_of = time_index * frames_dev + rim_pos // (rim_rows * col_count) - 1
    row_of = band_index * rows_dev + (rim_pos // col_count) % rim_rows - 1
    live = (
        (frame_of >= 0)
        & (frame_of < time_count * frames_dev)
        & (row_of >= 0)
        & (row_of < height)
    ).reshape(1, rim_n)
    gaps = gap_table(live, *dims)
    reach = jnp.stack([reach_time, reach_height, reach_width]).astype(jnp.int32)

    def own_spec(which):
        return pl.BlockSpec((None, own_n, DH * PER_STEP), lambda h, r: (which, 0, h))

    def rim_spec(which):
        return pl.BlockSpec((None, rim_n, DH * PER_STEP), lambda h, r: (which, 0, h))

    live_spec = pl.BlockSpec((3, own_n, rim_n), lambda h, r: (0, 0, 0))
    pair_spec = pl.BlockSpec((2, own_n, DH * PER_STEP), lambda h, r: (0, 0, h))
    stat_spec = pl.BlockSpec((PER_STEP, own_n, 1), lambda h, r: (h, 0, 0))

    og, lse, dots = pl.pallas_call(
        make_query_kernel(),
        grid_spec=pltpu.PrefetchScalarGridSpec(
            num_scalar_prefetch=1,
            grid=(heads // PER_STEP,),
            in_specs=[own_spec(2), own_spec(3), rim_spec(0), rim_spec(1), live_spec],
            out_specs=[pair_spec, stat_spec, stat_spec],
        ),
        out_shape=[
            jax.ShapeDtypeStruct((2, own_n, features), jnp.bfloat16),
            jax.ShapeDtypeStruct((heads, own_n, 1), jnp.float32),
            jax.ShapeDtypeStruct((heads, own_n, 1), jnp.float32),
        ],
    )(reach, own_flat, own_flat, kv_rim, kv_rim, gaps)

    def back_to_columns(pair):
        shaped = pair.reshape(2, frames_dev, rows_dev, col_count, features)
        return lax.all_to_all(shaped, "ulysses", split_axis=3, concat_axis=2, tiled=True)

    og_back = back_to_columns(og)

    statistics = jnp.stack([lse, dots]).reshape(2, heads, frames_dev, rows_dev, col_count)
    stat_rim = with_halo(statistics, (("tm", 2), ("ulysses", 3)), 1).reshape(2, heads, 1, rim_n)
    stat_rim_spec = [
        pl.BlockSpec((None, PER_STEP, 1, rim_n), lambda h, r, w=w: (w, h, 0, 0)) for w in range(2)
    ]
    gkv = pl.pallas_call(
        make_key_kernel(),
        grid_spec=pltpu.PrefetchScalarGridSpec(
            num_scalar_prefetch=1,
            grid=(heads // PER_STEP,),
            in_specs=[own_spec(0), own_spec(1), rim_spec(0), rim_spec(1)]
            + stat_rim_spec
            + [live_spec],
            out_specs=pair_spec,
        ),
        out_shape=jax.ShapeDtypeStruct((2, own_n, features), jnp.bfloat16),
    )(reach, own_flat, own_flat, qd_rim, qd_rim, stat_rim, stat_rim, gaps)
    gkv_back = back_to_columns(gkv)
    return (og_back[0], og_back[1], gkv_back[0], gkv_back[1])


def solution(mesh):
    in_specs = (
        P("tm", None, "ulysses", None),
        P("tm", None, "ulysses", None),
        P("tm", None, "ulysses", None),
        P("tm", None, "ulysses", None),
        P(),
        P(),
        P(),
    )
    out_specs = (
        P("tm", None, "ulysses", None),
        P("tm", None, "ulysses", None),
        P("tm", None, "ulysses", None),
        P("tm", None, "ulysses", None),
    )
    return jax.shard_map(body, mesh=mesh, in_specs=in_specs, out_specs=out_specs, check_vma=False)
```
